256 devices in a mesh: tok: 32 (over x, z), hid: 8 (over y, core).
Axes of the slice: x: 4, y: 4, z: 8, core: 2. Of those that a mesh axis runs over, the one named last changes fastest.
Arguments:
- tokens: bfloat16 [16384, 5376], P('tok', 'hid'), may hold values from -6 to 6
- norm_gain: bfloat16 [1, 5376], P(None, 'hid'), may hold values from 0.099609375 to 1.8984375
- w_query: bfloat16 [5376, 4096], P('tok', 'hid'), may hold values from -2 to 2
- w_key: bfloat16 [5376, 2048], P('tok', 'hid'), may hold values from -1 to 1
- value_matrix: bfloat16 [5376, 2048], P('tok', 'hid'), may hold values from -0.078125 to 0.078125
- q_norm_gain: bfloat16 [1, 128], replicated, may hold values from 0.1 to 8
- k_norm_gain: bfloat16 [1, 128], replicated, may hold values from 0.1 to 8
- w_out: bfloat16 [4096, 5376], P('hid'), may hold values from -0.125 to 0.125
Outputs:
- attended: bfloat16 [16384, 5376], P('tok', 'hid')
The draws below stay inside these ranges and needn't reach their ends.
All inputs are finite; a program needn't handle non-finite values.
Results may differ from the reference program's by a relative error of at most 0.017.
Values may be sent and summed in bfloat16 or wider, within the bound.
No kernel may reach another device: no remote copies, remote signals or barrier semaphores. Data moves between devices by JAX's collectives and lax.ppermute only.
A program may use at most 64 MiB of HBM per device.

```python
import math
import jax
import jax.numpy as jnp
from jax import lax

MODEL_WIDTH = 5376
QUERY_HEADS = 32
KEY_VALUE_HEADS = 16
HEAD_SIZE = 128
WINDOW = 1024
TOKENS_PER_PART = 512
TOKENS = 16384
REACH = 2
N_HID = 8


def draw_pair(key):
    key_matrix = jax.random.truncated_normal(jax.random.fold_in(key, 101), -4.0, 4.0, (MODEL_WIDTH, KEY_VALUE_HEADS * HEAD_SIZE), jnp.float32) / math.sqrt(MODEL_WIDTH)
    query_weight = jax.random.truncated_normal(jax.random.fold_in(key, 102), -4.0, 4.0, (MODEL_WIDTH, QUERY_HEADS * HEAD_SIZE), jnp.float32) / math.sqrt(MODEL_WIDTH)
    return (query_weight, key_matrix)


def draw_w_query(key, part):
    return draw_pair(key)[0].astype(jnp.bfloat16)


def draw_w_key(key, part):
    return draw_pair(key)[1].astype(jnp.bfloat16)


def draw_head_gain(key, salt):
    inner = jax.random.fold_in(key, salt)
    gain = 1.0 + 0.18 * jax.random.truncated_normal(inner, -4.5, 4.5, (1, HEAD_SIZE), jnp.float32)
    return gain.astype(jnp.bfloat16)


def draw_q_norm_gain(key, part):
    return draw_head_gain(key, 201)


def draw_k_norm_gain(key, part):
    return draw_head_gain(key, 202)


def with_spikes(drawn, key, source, target, blocks, factor):
    owner, partner = [(jnp.arange(drawn.shape[dim]) // (drawn.shape[dim] // blocks)).reshape([-1 if axis == dim else 1 for axis in range(drawn.ndim)]) for dim in (source, target)]
    chosen = jax.random.permutation(key, blocks)[partner]
    strong = (owner == chosen) | (owner == (partner + blocks // 2) % blocks)
    return jnp.where(strong, factor * drawn, drawn)


def steps_of(key, extent, pieces, least, largest):
    loudness = 1.0
    for axis_at, shards_of in pieces:
        draws = jax.random.uniform(jax.random.fold_in(jax.random.fold_in(key, 6), axis_at), (shards_of,), jnp.float32, least / len(pieces), largest / len(pieces))
        loudness = loudness * jnp.repeat(jnp.exp(draws), extent[axis_at] // shards_of).reshape((-1,) + (1,) * (len(extent) - 1 - axis_at))
    return loudness


def noise(own_key, dims, spread, limit, split=(), kind=jnp.bfloat16):
    array = spread * jax.random.normal(own_key, dims, jnp.float32)
    if split:
        array = array * steps_of(own_key, dims, split, -0.22, 0.18)
    return jnp.clip(array, -limit, limit).astype(kind)


def heavy_noise(own_key, extent, deviation, reach, pieces, heavy, kind=jnp.bfloat16):
    result = deviation * jax.random.normal(own_key, extent, jnp.float32)
    if pieces:
        result = result * steps_of(own_key, extent, pieces, -0.22, 0.18)
    return jnp.clip(with_spikes(result, jax.random.fold_in(own_key, 3), *heavy), -reach, reach).astype(kind)


def setup_inputs(seed: int = 0) -> dict:
    seeds = jax.random.split(jax.random.key(seed), 9)
    return {
        "tokens": noise(seeds[0], (TOKENS, MODEL_WIDTH), 1.0, 6.0, ((0, 32), (1, 8))),
        "norm_gain": jnp.clip(1.0 + 0.18 * jax.random.normal(seeds[1], (1, MODEL_WIDTH), jnp.float32), 0.099609375, 1.8984375).astype(jnp.bfloat16),
        "w_query": draw_w_query(jax.random.fold_in(seeds[8], 71), 0),
        "w_key": draw_w_key(jax.random.fold_in(seeds[8], 71), 0),
        "value_matrix": noise(seeds[4], (MODEL_WIDTH, KEY_VALUE_HEADS * HEAD_SIZE), MODEL_WIDTH ** -0.5, 0.078125, ((0, 32), (1, 8))),
        "q_norm_gain": draw_q_norm_gain(jax.random.fold_in(seeds[8], 71), 0),
        "k_norm_gain": draw_k_norm_gain(jax.random.fold_in(seeds[8], 71), 0),
        "w_out": heavy_noise(seeds[7], (QUERY_HEADS * HEAD_SIZE, MODEL_WIDTH), (QUERY_HEADS * HEAD_SIZE) ** -0.5, 0.125, ((0, 8),), (0, 1, 8, 2.0)),
    }


score_scale = 168.0 ** (-0.5)

def head_norm(field, gain):
    count = field.shape[0]
    heads = field.reshape(count, -1, HEAD_SIZE)
    mean_square = lax.optimization_barrier(jnp.mean(heads * heads, axis=-1, keepdims=True))
    scaled = heads * lax.rsqrt(mean_square + 1e-06) * gain.astype(jnp.float32).reshape(1, 1, HEAD_SIZE)
    return scaled.reshape(count, -1)

def rotate(field, positions):
    count = field.shape[0]
    heads = field.reshape(count, -1, HEAD_SIZE)
    half = HEAD_SIZE // 2
    inverse = jnp.exp(-math.log(10000.0) * jnp.arange(half, dtype=jnp.float32) * 2.0 / HEAD_SIZE)
    angles = positions.astype(jnp.float32)[:, None] * inverse[None, :]
    cosine = jnp.cos(angles)[:, None, :]
    sine = jnp.sin(angles)[:, None, :]
    first = heads[..., :half]
    second = heads[..., half:]
    turned = jnp.concatenate([first * cosine - second * sine, second * cosine + first * sine], axis=-1)
    return turned.reshape(count, -1)

def reference(tokens, norm_gain, w_query, w_key, value_matrix, q_norm_gain, k_norm_gain, w_out):
    values32 = tokens.astype(jnp.float32)
    scale_rows = lax.rsqrt(lax.optimization_barrier(jnp.mean(values32 * values32, axis=1, keepdims=True)) + 1e-06)
    normed = (values32 * scale_rows * norm_gain.astype(jnp.float32)).astype(jnp.bfloat16)
    positions = jnp.arange(TOKENS, dtype=jnp.int32)
    query_raw = jnp.dot(normed, w_query, preferred_element_type=jnp.float32)
    key_raw = jnp.dot(normed, w_key, preferred_element_type=jnp.float32)
    query = rotate(head_norm(query_raw, q_norm_gain), positions).astype(jnp.bfloat16)
    key = rotate(head_norm(key_raw, k_norm_gain), positions).astype(jnp.bfloat16)
    value_rows = jnp.dot(normed, value_matrix, preferred_element_type=jnp.float32).astype(jnp.bfloat16)
    leading_part = REACH * TOKENS_PER_PART
    padded_keys = jnp.concatenate([jnp.zeros((leading_part, KEY_VALUE_HEADS * HEAD_SIZE), jnp.bfloat16), key], axis=0)
    padded_values = jnp.concatenate([jnp.zeros((leading_part, KEY_VALUE_HEADS * HEAD_SIZE), jnp.bfloat16), value_rows], axis=0)
    query_group_count = QUERY_HEADS // KEY_VALUE_HEADS
    window_extent = (REACH + 1) * TOKENS_PER_PART

    def one_block(block):
        start = (block * TOKENS_PER_PART).astype(jnp.int32)
        query_tile_rows = lax.dynamic_slice_in_dim(query, start, TOKENS_PER_PART, 0)
        nearby_keys = lax.dynamic_slice_in_dim(padded_keys, start, window_extent, 0)
        nearby_values = lax.dynamic_slice_in_dim(padded_values, start, window_extent, 0)
        query_pos = start + jnp.arange(TOKENS_PER_PART, dtype=jnp.int32)
        key_pos = start - leading_part + jnp.arange(window_extent, dtype=jnp.int32)
        query_four_axes = query_tile_rows.reshape(TOKENS_PER_PART, KEY_VALUE_HEADS, query_group_count, HEAD_SIZE).astype(jnp.float32)
        keys_three_axes = nearby_keys.reshape(window_extent, KEY_VALUE_HEADS, HEAD_SIZE).astype(jnp.float32)
        values_three_axes = nearby_values.reshape(window_extent, KEY_VALUE_HEADS, HEAD_SIZE).astype(jnp.float32)
        scores = jnp.einsum('tkgd,skd->kgts', query_four_axes, keys_three_axes) * score_scale
        allowed = (key_pos[None, :] <= query_pos[:, None]) & (key_pos[None, :] > query_pos[:, None] - WINDOW) & (key_pos[None, :] >= 0)
        masked = jnp.where(allowed, scores, -1e+30)
        top = lax.optimization_barrier(jnp.max(masked, axis=-1, keepdims=True))
        weights = jnp.where(allowed, jnp.exp(masked - top), 0.0)
        total = lax.optimization_barrier(jnp.sum(weights, axis=-1))
        probs = weights.astype(jnp.bfloat16).astype(jnp.float32)
        mixed = jnp.einsum('kgts,skd->tkgd', probs, values_three_axes)
        mixed = mixed / jnp.transpose(total, (2, 0, 1))[..., None]
        return mixed.reshape(TOKENS_PER_PART, QUERY_HEADS * HEAD_SIZE).astype(jnp.bfloat16)
    blocks = lax.map(one_block, jnp.arange(TOKENS // TOKENS_PER_PART, dtype=jnp.int32))
    heads_out = blocks.reshape(TOKENS, QUERY_HEADS * HEAD_SIZE)
    block_width = QUERY_HEADS * HEAD_SIZE // N_HID
    summed = jnp.zeros((TOKENS, MODEL_WIDTH), jnp.float32)
    for block in range(N_HID):
        part = jnp.dot(heads_out[:, block * block_width:(block + 1) * block_width], w_out[block * block_width:(block + 1) * block_width], preferred_element_type=jnp.float32)
        rounded = lax.optimization_barrier(part.astype(jnp.bfloat16))
        summed = summed + rounded.astype(jnp.float32)
    return summed.astype(jnp.bfloat16)
```

```python
import math

import jax
import jax.numpy as jnp
from jax import lax
from jax.sharding import PartitionSpec as P

HEAD_SIZE = 128
WINDOW = 1024


score_scale = 168.0 ** (-0.5)


def shifted(value, axis, steps):
    count = lax.axis_size(axis)
    leading, last = (max(0, -steps), min(count, count - steps))
    return lax.ppermute(value, axis, [(source, source + steps) for source in range(leading, last)])


def head_norm(field, gain):
    count = field.shape[0]
    heads = field.reshape(count, -1, HEAD_SIZE)
    mean_square = jnp.mean(heads * heads, axis=-1, keepdims=True)
    scaled = (
        heads * lax.rsqrt(mean_square + 1e-06) * gain.astype(jnp.float32).reshape(1, 1, HEAD_SIZE)
    )
    return scaled.reshape(count, -1)


def rotate(field, positions):
    count = field.shape[0]
    heads = field.reshape(count, -1, HEAD_SIZE)
    half = HEAD_SIZE // 2
    inverse = jnp.exp(-math.log(10000.0) * jnp.arange(half, dtype=jnp.float32) * 2.0 / HEAD_SIZE)
    angles = positions.astype(jnp.float32)[:, None] * inverse[None, :]
    cosine = jnp.cos(angles)[:, None, :]
    sine = jnp.sin(angles)[:, None, :]
    first = heads[..., :half]
    second = heads[..., half:]
    turned = jnp.concatenate(
        [first * cosine - second * sine, second * cosine + first * sine], axis=-1
    )
    return turned.reshape(count, -1)


def local(tokens, norm_gain, w_query, w_key, value_matrix, q_norm_gain, k_norm_gain, w_out):
    rows = tokens.shape[0]
    with_gain = jnp.concatenate([tokens, norm_gain], axis=0)
    gathered_all = lax.all_gather(with_gain, "hid", axis=1, tiled=True)
    gathered, gain_row = gathered_all[:rows], gathered_all[rows:]
    values32 = gathered.astype(jnp.float32)
    scale_rows = lax.rsqrt(jnp.mean(values32 * values32, axis=1, keepdims=True) + 1e-06)
    normed = (values32 * scale_rows * gain_row.astype(jnp.float32)).astype(jnp.bfloat16)
    width_query = w_query.shape[1]
    width_kv = w_key.shape[1]
    stacked = lax.all_gather(
        jnp.concatenate([w_query, w_key, value_matrix], axis=1), "tok", axis=0, tiled=True
    )
    pieces = (
        stacked[:, :width_query],
        stacked[:, width_query : width_query + width_kv],
        stacked[:, width_query + width_kv :],
    )
    query_raw, key_raw, value_raw = tuple(
        (jnp.dot(normed, piece, preferred_element_type=jnp.float32) for piece in pieces)
    )
    tok_index = lax.axis_index("tok")
    positions = tok_index * rows + jnp.arange(rows, dtype=jnp.int32)
    query = rotate(head_norm(query_raw, q_norm_gain), positions).astype(jnp.bfloat16)
    key = rotate(head_norm(key_raw, k_norm_gain), positions).astype(jnp.bfloat16)
    value_rows = value_raw.astype(jnp.bfloat16)
    joined = jnp.concatenate([key, value_rows], axis=1)
    reach = (WINDOW - 1 + rows - 1) // rows
    earlier = []
    moving = joined
    for offset in range(reach):
        moving = shifted(moving, "tok", 1)
        earlier = [moving] + earlier
    window_kv = jnp.concatenate(earlier + [joined], axis=0)
    window_extent = window_kv.shape[0]
    key_pos = (tok_index - reach) * rows + jnp.arange(window_extent, dtype=jnp.int32)
    kv_heads = width_kv // HEAD_SIZE
    query_group_count = width_query // HEAD_SIZE // kv_heads
    query_four_axes = query.reshape(rows, kv_heads, query_group_count, HEAD_SIZE)
    keys_three_axes = window_kv[:, :width_kv].reshape(window_extent, kv_heads, HEAD_SIZE)
    values_three_axes = window_kv[:, width_kv:].reshape(window_extent, kv_heads, HEAD_SIZE)
    scores = (
        jnp.einsum(
            "tkgd,skd->kgts", query_four_axes, keys_three_axes, preferred_element_type=jnp.float32
        )
        * score_scale
    )
    allowed = (
        (key_pos[None, :] <= positions[:, None])
        & (key_pos[None, :] > positions[:, None] - WINDOW)
        & (key_pos[None, :] >= 0)
    )
    masked = jnp.where(allowed, scores, -1e30)
    top = jnp.max(masked, axis=-1, keepdims=True)
    weights = jnp.where(allowed, jnp.exp(masked - top), 0.0)
    total = jnp.sum(weights, axis=-1)
    probs = weights.astype(jnp.bfloat16)
    mixed = jnp.einsum(
        "kgts,skd->tkgd", probs, values_three_axes, preferred_element_type=jnp.float32
    )
    mixed = mixed / jnp.transpose(total, (2, 0, 1))[..., None]
    heads_out = mixed.reshape(rows, width_query).astype(jnp.bfloat16)
    partial_value = jnp.dot(heads_out, w_out, preferred_element_type=jnp.float32)
    return lax.psum_scatter(
        partial_value.astype(jnp.bfloat16), "hid", scatter_dimension=1, tiled=True
    )


def solution(mesh):
    in_specs = (
        P("tok", "hid"),
        P(None, "hid"),
        P("tok", "hid"),
        P("tok", "hid"),
        P("tok", "hid"),
        P(),
        P(),
        P("hid", None),
    )
    out_specs = P("tok", "hid")
    return jax.shard_map(local, mesh=mesh, in_specs=in_specs, out_specs=out_specs, check_vma=False)
```

```python
import math

import jax
import jax.numpy as jnp
from jax import lax
from jax.sharding import PartitionSpec as P

HEAD_SIZE = 128
WINDOW = 1024


score_scale = 168.0 ** (-0.5)


def shifted(value, axis, steps):
    count = lax.axis_size(axis)
    leading, last = (max(0, -steps), min(count, count - steps))
    return lax.ppermute(value, axis, [(source, source + steps) for source in range(leading, last)])


def head_norm(field, gain):
    count = field.shape[0]
    heads = field.reshape(count, -1, HEAD_SIZE)
    mean_square = jnp.mean(heads * heads, axis=-1, keepdims=True)
    scaled = (
        heads * lax.rsqrt(mean_square + 1e-06) * gain.astype(jnp.float32).reshape(1, 1, HEAD_SIZE)
    )
    return scaled.reshape(count, -1)


def rotate(field, positions):
    count = field.shape[0]
    heads = field.reshape(count, -1, HEAD_SIZE)
    half = HEAD_SIZE // 2
    inverse = jnp.exp(-math.log(10000.0) * jnp.arange(half, dtype=jnp.float32) * 2.0 / HEAD_SIZE)
    angles = positions.astype(jnp.float32)[:, None] * inverse[None, :]
    cosine = jnp.cos(angles)[:, None, :]
    sine = jnp.sin(angles)[:, None, :]
    first = heads[..., :half]
    second = heads[..., half:]
    turned = jnp.concatenate(
        [first * cosine - second * sine, second * cosine + first * sine], axis=-1
    )
    return turned.reshape(count, -1)


def local(tokens, norm_gain, w_query, w_key, value_matrix, q_norm_gain, k_norm_gain, w_out):
    rows = tokens.shape[0]
    with_gain = jnp.concatenate([tokens, norm_gain], axis=0)
    n_hid = lax.axis_size("hid")
    hid_index = lax.axis_index("hid")
    received = [with_gain] + [
        lax.ppermute(with_gain, "hid", [(i, (i + k) % n_hid) for i in range(n_hid)])
        for k in range(1, n_hid)
    ]
    by_shift = jnp.stack(received)
    ordered = jnp.take(by_shift, (hid_index - jnp.arange(n_hid)) % n_hid, axis=0)
    gathered_all = jnp.transpose(ordered, (1, 0, 2)).reshape(rows + 1, -1)
    gathered, gain_row = gathered_all[:rows], gathered_all[rows:]
    values32 = gathered.astype(jnp.float32)
    scale_rows = lax.rsqrt(jnp.mean(values32 * values32, axis=1, keepdims=True) + 1e-06)
    normed = (values32 * scale_rows * gain_row.astype(jnp.float32)).astype(jnp.bfloat16)
    width_query = w_query.shape[1]
    width_kv = w_key.shape[1]
    stacked = lax.all_gather(
        jnp.concatenate([w_query, w_key, value_matrix], axis=1), "tok", axis=0, tiled=True
    )
    pieces = (
        stacked[:, :width_query],
        stacked[:, width_query : width_query + width_kv],
        stacked[:, width_query + width_kv :],
    )
    query_raw, key_raw, value_raw = tuple(
        (jnp.dot(normed, piece, preferred_element_type=jnp.float32) for piece in pieces)
    )
    tok_index = lax.axis_index("tok")
    positions = tok_index * rows + jnp.arange(rows, dtype=jnp.int32)
    query = rotate(head_norm(query_raw, q_norm_gain), positions).astype(jnp.bfloat16)
    key = rotate(head_norm(key_raw, k_norm_gain), positions).astype(jnp.bfloat16)
    value_rows = value_raw.astype(jnp.bfloat16)
    joined = jnp.concatenate([key, value_rows], axis=1)
    reach = (WINDOW - 1 + rows - 1) // rows
    earlier = [shifted(joined, "tok", offset) for offset in range(reach, 0, -1)]
    window_kv = jnp.concatenate(earlier + [joined], axis=0)
    window_extent = window_kv.shape[0]
    key_pos = (tok_index - reach) * rows + jnp.arange(window_extent, dtype=jnp.int32)
    kv_heads = width_kv // HEAD_SIZE
    query_group_count = width_query // HEAD_SIZE // kv_heads
    query_four_axes = query.reshape(rows, kv_heads, query_group_count, HEAD_SIZE)
    keys_three_axes = window_kv[:, :width_kv].reshape(window_extent, kv_heads, HEAD_SIZE)
    values_three_axes = window_kv[:, width_kv:].reshape(window_extent, kv_heads, HEAD_SIZE)
    scores = (
        jnp.einsum(
            "tkgd,skd->kgts", query_four_axes, keys_three_axes, preferred_element_type=jnp.float32
        )
        * score_scale
    )
    allowed = (
        (key_pos[None, :] <= positions[:, None])
        & (key_pos[None, :] > positions[:, None] - WINDOW)
        & (key_pos[None, :] >= 0)
    )
    masked = jnp.where(allowed, scores, -1e30)
    top = jnp.max(masked, axis=-1, keepdims=True)
    weights = jnp.where(allowed, jnp.exp(masked - top), 0.0)
    total = jnp.sum(weights, axis=-1)
    probs = weights.astype(jnp.bfloat16)
    mixed = jnp.einsum(
        "kgts,skd->tkgd", probs, values_three_axes, preferred_element_type=jnp.float32
    )
    mixed = mixed / jnp.transpose(total, (2, 0, 1))[..., None]
    heads_out = mixed.reshape(rows, width_query).astype(jnp.bfloat16)
    partial_value = jnp.dot(heads_out, w_out, preferred_element_type=jnp.float32)
    return lax.psum_scatter(
        partial_value.astype(jnp.bfloat16), "hid", scatter_dimension=1, tiled=True
    )


def solution(mesh):
    in_specs = (
        P("tok", "hid"),
        P(None, "hid"),
        P("tok", "hid"),
        P("tok", "hid"),
        P("tok", "hid"),
        P(),
        P(),
        P("hid", None),
    )
    out_specs = P("tok", "hid")
    return jax.shard_map(local, mesh=mesh, in_specs=in_specs, out_specs=out_specs, check_vma=False)
```

```python
import math

import jax
import jax.numpy as jnp
from jax import lax
from jax.sharding import PartitionSpec as P

HEAD_SIZE = 128
WINDOW = 1024


score_scale = 168.0 ** (-0.5)


def shifted(value, axis, steps):
    count = lax.axis_size(axis)
    leading, last = (max(0, -steps), min(count, count - steps))
    return lax.ppermute(value, axis, [(source, source + steps) for source in range(leading, last)])


def head_norm(field, gain):
    count = field.shape[0]
    heads = field.reshape(count, -1, HEAD_SIZE)
    mean_square = jnp.mean(heads * heads, axis=-1, keepdims=True)
    scaled = (
        heads * lax.rsqrt(mean_square + 1e-06) * gain.astype(jnp.float32).reshape(1, 1, HEAD_SIZE)
    )
    return scaled.reshape(count, -1)


def rotate(field, positions):
    count = field.shape[0]
    heads = field.reshape(count, -1, HEAD_SIZE)
    half = HEAD_SIZE // 2
    inverse = jnp.exp(-math.log(10000.0) * jnp.arange(half, dtype=jnp.float32) * 2.0 / HEAD_SIZE)
    angles = positions.astype(jnp.float32)[:, None] * inverse[None, :]
    cosine = jnp.cos(angles)[:, None, :]
    sine = jnp.sin(angles)[:, None, :]
    first = heads[..., :half]
    second = heads[..., half:]
    turned = jnp.concatenate(
        [first * cosine - second * sine, second * cosine + first * sine], axis=-1
    )
    return turned.reshape(count, -1)


def local(tokens, norm_gain, w_query, w_key, value_matrix, q_norm_gain, k_norm_gain, w_out):
    rows = tokens.shape[0]
    with_gain = jnp.concatenate([tokens, norm_gain], axis=0)
    n_hid = lax.axis_size("hid")
    hid_index = lax.axis_index("hid")
    received = [with_gain] + [
        lax.ppermute(with_gain, "hid", [(i, (i + k) % n_hid) for i in range(n_hid)])
        for k in range(1, n_hid)
    ]
    by_shift = jnp.stack(received)
    ordered = jnp.take(by_shift, (hid_index - jnp.arange(n_hid)) % n_hid, axis=0)
    values32 = ordered[:, :rows].astype(jnp.float32)
    gain_rows = ordered[:, rows:].astype(jnp.float32)
    mean_square = jnp.sum(values32 * values32, axis=(0, 2)) / (n_hid * values32.shape[2])
    scale_rows = lax.rsqrt(mean_square + 1e-06)[None, :, None]
    normed = (values32 * scale_rows * gain_rows).astype(jnp.bfloat16)
    width_query = w_query.shape[1]
    width_kv = w_key.shape[1]
    stacked = lax.all_gather(
        jnp.concatenate([w_query, w_key, value_matrix], axis=1), "tok", axis=0, tiled=True
    )
    projected = jnp.einsum(
        "jrc,jcn->rn",
        normed,
        stacked.reshape(n_hid, normed.shape[2], stacked.shape[1]),
        preferred_element_type=jnp.float32,
    )
    query_raw = projected[:, :width_query]
    key_raw = projected[:, width_query : width_query + width_kv]
    value_raw = projected[:, width_query + width_kv :]
    tok_index = lax.axis_index("tok")
    positions = tok_index * rows + jnp.arange(rows, dtype=jnp.int32)
    query = rotate(head_norm(query_raw, q_norm_gain), positions).astype(jnp.bfloat16)
    key = rotate(head_norm(key_raw, k_norm_gain), positions).astype(jnp.bfloat16)
    value_rows = value_raw.astype(jnp.bfloat16)
    joined = jnp.concatenate([key, value_rows], axis=1)
    reach = (WINDOW - 1 + rows - 1) // rows
    earlier = [shifted(joined, "tok", offset) for offset in range(reach, 0, -1)]
    window_kv = jnp.concatenate(earlier + [joined], axis=0)
    window_extent = window_kv.shape[0]
    key_pos = (tok_index - reach) * rows + jnp.arange(window_extent, dtype=jnp.int32)
    kv_heads = width_kv // HEAD_SIZE
    query_group_count = width_query // HEAD_SIZE // kv_heads
    query_four_axes = query.reshape(rows, kv_heads, query_group_count, HEAD_SIZE)
    keys_three_axes = window_kv[:, :width_kv].reshape(window_extent, kv_heads, HEAD_SIZE)
    values_three_axes = window_kv[:, width_kv:].reshape(window_extent, kv_heads, HEAD_SIZE)
    scores = (
        jnp.einsum(
            "tkgd,skd->kgts", query_four_axes, keys_three_axes, preferred_element_type=jnp.float32
        )
        * score_scale
    )
    allowed = (
        (key_pos[None, :] <= positions[:, None])
        & (key_pos[None, :] > positions[:, None] - WINDOW)
        & (key_pos[None, :] >= 0)
    )
    masked = jnp.where(allowed, scores, -1e30)
    top = jnp.max(masked, axis=-1, keepdims=True)
    weights = jnp.where(allowed, jnp.exp(masked - top), 0.0)
    total = jnp.sum(weights, axis=-1)
    probs = weights.astype(jnp.bfloat16)
    mixed = jnp.einsum(
        "kgts,skd->tkgd", probs, values_three_axes, preferred_element_type=jnp.float32
    )
    mixed = mixed / jnp.transpose(total, (2, 0, 1))[..., None]
    heads_out = mixed.reshape(rows, width_query).astype(jnp.bfloat16)
    partial_value = jnp.dot(heads_out, w_out, preferred_element_type=jnp.float32)
    return lax.psum_scatter(
        partial_value.astype(jnp.bfloat16), "hid", scatter_dimension=1, tiled=True
    )


def solution(mesh):
    in_specs = (
        P("tok", "hid"),
        P(None, "hid"),
        P("tok", "hid"),
        P("tok", "hid"),
        P("tok", "hid"),
        P(),
        P(),
        P("hid", None),
    )
    out_specs = P("tok", "hid")
    return jax.shard_map(local, mesh=mesh, in_specs=in_specs, out_specs=out_specs, check_vma=False)
```

```python
import math

import jax
import jax.numpy as jnp
from jax import lax
from jax.sharding import PartitionSpec as P

HEAD_SIZE = 128
WINDOW = 1024


score_scale = 168.0 ** (-0.5)


def shifted(value, axis, steps):
    count = lax.axis_size(axis)
    leading, last = (max(0, -steps), min(count, count - steps))
    return lax.ppermute(value, axis, [(source, source + steps) for source in range(leading, last)])


def head_norm(field, gain):
    count = field.shape[0]
    heads = field.reshape(count, -1, HEAD_SIZE)
    mean_square = jnp.mean(heads * heads, axis=-1, keepdims=True)
    scaled = (
        heads * lax.rsqrt(mean_square + 1e-06) * gain.astype(jnp.float32).reshape(1, 1, HEAD_SIZE)
    )
    return scaled.reshape(count, -1)


def rotate(field, positions):
    count = field.shape[0]
    heads = field.reshape(count, -1, HEAD_SIZE)
    half = HEAD_SIZE // 2
    inverse = jnp.exp(-math.log(10000.0) * jnp.arange(half, dtype=jnp.float32) * 2.0 / HEAD_SIZE)
    angles = positions.astype(jnp.float32)[:, None] * inverse[None, :]
    cosine = jnp.cos(angles)[:, None, :]
    sine = jnp.sin(angles)[:, None, :]
    first = heads[..., :half]
    second = heads[..., half:]
    turned = jnp.concatenate(
        [first * cosine - second * sine, second * cosine + first * sine], axis=-1
    )
    return turned.reshape(count, -1)


def local(tokens, norm_gain, w_query, w_key, value_matrix, q_norm_gain, k_norm_gain, w_out):
    rows = tokens.shape[0]
    with_gain = jnp.concatenate([tokens, norm_gain], axis=0)
    n_hid = lax.axis_size("hid")
    hid_index = lax.axis_index("hid")
    received = [with_gain] + [
        lax.ppermute(with_gain, "hid", [(i, (i + k) % n_hid) for i in range(n_hid)])
        for k in range(1, n_hid)
    ]
    by_shift = jnp.stack(received)
    ordered = jnp.take(by_shift, (hid_index - jnp.arange(n_hid)) % n_hid, axis=0)
    values32 = ordered[:, :rows].astype(jnp.float32)
    gain_rows = ordered[:, rows:].astype(jnp.float32)
    mean_square = jnp.sum(values32 * values32, axis=(0, 2)) / (n_hid * values32.shape[2])
    scale_rows = lax.rsqrt(mean_square + 1e-06)[None, :, None]
    normed = (values32 * scale_rows * gain_rows).astype(jnp.bfloat16)
    width_query = w_query.shape[1]
    width_kv = w_key.shape[1]
    stacked = lax.all_gather(
        jnp.concatenate([w_query, w_key, value_matrix], axis=1), "tok", axis=0, tiled=True
    )
    weights3 = stacked.reshape(n_hid, normed.shape[2], stacked.shape[1])
    projected_kv = jnp.einsum(
        "jrc,jcn->rn", normed, weights3[:, :, width_query:], preferred_element_type=jnp.float32
    )
    key_raw = projected_kv[:, :width_kv]
    value_raw = projected_kv[:, width_kv:]
    tok_index = lax.axis_index("tok")
    positions = tok_index * rows + jnp.arange(rows, dtype=jnp.int32)
    key = rotate(head_norm(key_raw, k_norm_gain), positions).astype(jnp.bfloat16)
    value_rows = value_raw.astype(jnp.bfloat16)
    joined = jnp.concatenate([key, value_rows], axis=1)
    reach = (WINDOW - 1 + rows - 1) // rows
    earlier = [shifted(joined, "tok", offset) for offset in range(reach, 0, -1)]
    normed_late, _ = lax.optimization_barrier((normed, joined))
    query_raw = jnp.einsum(
        "jrc,jcn->rn", normed_late, weights3[:, :, :width_query], preferred_element_type=jnp.float32
    )
    query = rotate(head_norm(query_raw, q_norm_gain), positions).astype(jnp.bfloat16)
    window_kv = jnp.concatenate(earlier + [joined], axis=0)
    window_extent = window_kv.shape[0]
    key_pos = (tok_index - reach) * rows + jnp.arange(window_extent, dtype=jnp.int32)
    kv_heads = width_kv // HEAD_SIZE
    query_group_count = width_query // HEAD_SIZE // kv_heads
    query_four_axes = query.reshape(rows, kv_heads, query_group_count, HEAD_SIZE)
    keys_three_axes = window_kv[:, :width_kv].reshape(window_extent, kv_heads, HEAD_SIZE)
    values_three_axes = window_kv[:, width_kv:].reshape(window_extent, kv_heads, HEAD_SIZE)
    scores = (
        jnp.einsum(
            "tkgd,skd->kgts", query_four_axes, keys_three_axes, preferred_element_type=jnp.float32
        )
        * score_scale
    )
    allowed = (
        (key_pos[None, :] <= positions[:, None])
        & (key_pos[None, :] > positions[:, None] - WINDOW)
        & (key_pos[None, :] >= 0)
    )
    masked = jnp.where(allowed, scores, -1e30)
    top = jnp.max(masked, axis=-1, keepdims=True)
    weights = jnp.where(allowed, jnp.exp(masked - top), 0.0)
    total = jnp.sum(weights, axis=-1)
    probs = weights.astype(jnp.bfloat16)
    mixed = jnp.einsum(
        "kgts,skd->tkgd", probs, values_three_axes, preferred_element_type=jnp.float32
    )
    mixed = mixed / jnp.transpose(total, (2, 0, 1))[..., None]
    heads_out = mixed.reshape(rows, width_query).astype(jnp.bfloat16)
    partial_value = jnp.dot(heads_out, w_out, preferred_element_type=jnp.float32)
    return lax.psum_scatter(
        partial_value.astype(jnp.bfloat16), "hid", scatter_dimension=1, tiled=True
    )


def solution(mesh):
    in_specs = (
        P("tok", "hid"),
        P(None, "hid"),
        P("tok", "hid"),
        P("tok", "hid"),
        P("tok", "hid"),
        P(),
        P(),
        P("hid", None),
    )
    out_specs = P("tok", "hid")
    return jax.shard_map(local, mesh=mesh, in_specs=in_specs, out_specs=out_specs, check_vma=False)
```

```python
import math

import jax
import jax.numpy as jnp
from jax import lax
from jax.sharding import PartitionSpec as P

HEAD_SIZE = 128
WINDOW = 1024
TOK = ("tx", "tz")
HID = ("hy", "hc")


score_scale = 168.0 ** (-0.5)


def shifted(value, axis, steps):
    count = lax.axis_size(axis)
    leading, last = (max(0, -steps), min(count, count - steps))
    return lax.ppermute(value, axis, [(source, source + steps) for source in range(leading, last)])


def head_norm(field, gain):
    count = field.shape[0]
    heads = field.reshape(count, -1, HEAD_SIZE)
    mean_square = jnp.mean(heads * heads, axis=-1, keepdims=True)
    scaled = (
        heads * lax.rsqrt(mean_square + 1e-06) * gain.astype(jnp.float32).reshape(1, 1, HEAD_SIZE)
    )
    return scaled.reshape(count, -1)


def rotate(field, positions):
    count = field.shape[0]
    heads = field.reshape(count, -1, HEAD_SIZE)
    half = HEAD_SIZE // 2
    inverse = jnp.exp(-math.log(10000.0) * jnp.arange(half, dtype=jnp.float32) * 2.0 / HEAD_SIZE)
    angles = positions.astype(jnp.float32)[:, None] * inverse[None, :]
    cosine = jnp.cos(angles)[:, None, :]
    sine = jnp.sin(angles)[:, None, :]
    first = heads[..., :half]
    second = heads[..., half:]
    turned = jnp.concatenate(
        [first * cosine - second * sine, second * cosine + first * sine], axis=-1
    )
    return turned.reshape(count, -1)


def local(tokens, norm_gain, w_query, w_key, value_matrix, q_norm_gain, k_norm_gain, w_out):
    rows = tokens.shape[0]
    with_gain = jnp.concatenate([tokens, norm_gain], axis=0)
    n_hid = lax.axis_size(HID)
    hid_index = lax.axis_index(HID)
    received = [with_gain] + [
        lax.ppermute(with_gain, HID, [(i, (i + k) % n_hid) for i in range(n_hid)])
        for k in range(1, n_hid)
    ]
    by_shift = jnp.stack(received)
    ordered = jnp.take(by_shift, (hid_index - jnp.arange(n_hid)) % n_hid, axis=0)
    values32 = ordered[:, :rows].astype(jnp.float32)
    gain_rows = ordered[:, rows:].astype(jnp.float32)
    mean_square = jnp.sum(values32 * values32, axis=(0, 2)) / (n_hid * values32.shape[2])
    scale_rows = lax.rsqrt(mean_square + 1e-06)[None, :, None]
    normed = (values32 * scale_rows * gain_rows).astype(jnp.bfloat16)
    width_query = w_query.shape[1]
    width_kv = w_key.shape[1]
    stacked = lax.all_gather(
        lax.all_gather(
            jnp.concatenate([w_query, w_key, value_matrix], axis=1), "tz", axis=0, tiled=True
        ),
        "tx",
        axis=0,
        tiled=True,
    )
    weights3 = stacked.reshape(n_hid, normed.shape[2], stacked.shape[1])
    projected_kv = jnp.einsum(
        "jrc,jcn->rn", normed, weights3[:, :, width_query:], preferred_element_type=jnp.float32
    )
    key_raw = projected_kv[:, :width_kv]
    value_raw = projected_kv[:, width_kv:]
    tok_index = lax.axis_index(TOK)
    positions = tok_index * rows + jnp.arange(rows, dtype=jnp.int32)
    key = rotate(head_norm(key_raw, k_norm_gain), positions).astype(jnp.bfloat16)
    value_rows = value_raw.astype(jnp.bfloat16)
    joined = jnp.concatenate([key, value_rows], axis=1)
    reach = (WINDOW - 1 + rows - 1) // rows
    earlier = [shifted(joined, TOK, offset) for offset in range(reach, 0, -1)]
    normed_late, _ = lax.optimization_barrier((normed, joined))
    query_raw = jnp.einsum(
        "jrc,jcn->rn", normed_late, weights3[:, :, :width_query], preferred_element_type=jnp.float32
    )
    query = rotate(head_norm(query_raw, q_norm_gain), positions).astype(jnp.bfloat16)
    window_kv = jnp.concatenate(earlier + [joined], axis=0)
    window_extent = window_kv.shape[0]
    key_pos = (tok_index - reach) * rows + jnp.arange(window_extent, dtype=jnp.int32)
    kv_heads = width_kv // HEAD_SIZE
    query_group_count = width_query // HEAD_SIZE // kv_heads
    query_four_axes = query.reshape(rows, kv_heads, query_group_count, HEAD_SIZE)
    keys_three_axes = window_kv[:, :width_kv].reshape(window_extent, kv_heads, HEAD_SIZE)
    values_three_axes = window_kv[:, width_kv:].reshape(window_extent, kv_heads, HEAD_SIZE)
    scores = (
        jnp.einsum(
            "tkgd,skd->kgts", query_four_axes, keys_three_axes, preferred_element_type=jnp.float32
        )
        * score_scale
    )
    allowed = (
        (key_pos[None, :] <= positions[:, None])
        & (key_pos[None, :] > positions[:, None] - WINDOW)
        & (key_pos[None, :] >= 0)
    )
    masked = jnp.where(allowed, scores, -1e30)
    top = jnp.max(masked, axis=-1, keepdims=True)
    weights = jnp.where(allowed, jnp.exp(masked - top), 0.0)
    total = jnp.sum(weights, axis=-1)
    probs = weights.astype(jnp.bfloat16)
    mixed = jnp.einsum(
        "kgts,skd->tkgd", probs, values_three_axes, preferred_element_type=jnp.float32
    )
    mixed = mixed / jnp.transpose(total, (2, 0, 1))[..., None]
    heads_out = mixed.reshape(rows, width_query).astype(jnp.bfloat16)
    partial_value = jnp.dot(heads_out, w_out, preferred_element_type=jnp.float32)
    return lax.psum_scatter(
        partial_value.astype(jnp.bfloat16), HID, scatter_dimension=1, tiled=True
    )


def solution(mesh):
    devices = mesh.devices
    n_x = len({d.coords[0] for d in devices.flat})
    n_y = len({d.coords[1] for d in devices.flat})
    split = jax.sharding.Mesh(
        devices.reshape(n_x, devices.shape[0] // n_x, n_y, devices.shape[1] // n_y),
        ("tx", "tz", "hy", "hc"),
    )
    in_specs = (
        P(TOK, HID),
        P(None, HID),
        P(TOK, HID),
        P(TOK, HID),
        P(TOK, HID),
        P(),
        P(),
        P(HID, None),
    )
    out_specs = P(TOK, HID)
    return jax.shard_map(local, mesh=split, in_specs=in_specs, out_specs=out_specs, check_vma=False)
```

```python
import math

import jax
import jax.numpy as jnp
from jax import lax
from jax.sharding import PartitionSpec as P

HEAD_SIZE = 128
WINDOW = 1024
TOK = ("tx", "tz")
HID = ("hy", "hc")


score_scale = 168.0 ** (-0.5)


def shifted(value, axis, steps):
    count = lax.axis_size(axis)
    leading, last = (max(0, -steps), min(count, count - steps))
    return lax.ppermute(value, axis, [(source, source + steps) for source in range(leading, last)])


def head_norm(field, gain):
    count = field.shape[0]
    heads = field.reshape(count, -1, HEAD_SIZE)
    mean_square = jnp.mean(heads * heads, axis=-1, keepdims=True)
    scaled = (
        heads * lax.rsqrt(mean_square + 1e-06) * gain.astype(jnp.float32).reshape(1, 1, HEAD_SIZE)
    )
    return scaled.reshape(count, -1)


def rotate(field, positions):
    count = field.shape[0]
    heads = field.reshape(count, -1, HEAD_SIZE)
    half = HEAD_SIZE // 2
    inverse = jnp.exp(-math.log(10000.0) * jnp.arange(half, dtype=jnp.float32) * 2.0 / HEAD_SIZE)
    angles = positions.astype(jnp.float32)[:, None] * inverse[None, :]
    cosine = jnp.cos(angles)[:, None, :]
    sine = jnp.sin(angles)[:, None, :]
    first = heads[..., :half]
    second = heads[..., half:]
    turned = jnp.concatenate(
        [first * cosine - second * sine, second * cosine + first * sine], axis=-1
    )
    return turned.reshape(count, -1)


def local(tokens, norm_gain, w_query, w_key, value_matrix, q_norm_gain, k_norm_gain, w_out):
    rows = tokens.shape[0]
    with_gain = jnp.concatenate([tokens, norm_gain], axis=0)
    n_hid = lax.axis_size(HID)
    hid_index = lax.axis_index(HID)
    received = [with_gain] + [
        lax.ppermute(with_gain, HID, [(i, (i + k) % n_hid) for i in range(n_hid)])
        for k in range(1, n_hid)
    ]
    by_shift = jnp.stack(received)
    ordered = jnp.take(by_shift, (hid_index - jnp.arange(n_hid)) % n_hid, axis=0)
    values32 = ordered[:, :rows].astype(jnp.float32)
    gain_rows = ordered[:, rows:].astype(jnp.float32)
    mean_square = jnp.sum(values32 * values32, axis=(0, 2)) / (n_hid * values32.shape[2])
    scale_rows = lax.rsqrt(mean_square + 1e-06)[None, :, None]
    normed = (values32 * scale_rows * gain_rows).astype(jnp.bfloat16)
    width_query = w_query.shape[1]
    width_kv = w_key.shape[1]
    stacked = lax.all_gather(
        jnp.concatenate([w_query, w_key, value_matrix], axis=1), TOK, axis=0, tiled=True
    )
    weights3 = stacked.reshape(n_hid, normed.shape[2], stacked.shape[1])
    projected_kv = jnp.einsum(
        "jrc,jcn->rn", normed, weights3[:, :, width_query:], preferred_element_type=jnp.float32
    )
    key_raw = projected_kv[:, :width_kv]
    value_raw = projected_kv[:, width_kv:]
    tok_index = lax.axis_index(TOK)
    positions = tok_index * rows + jnp.arange(rows, dtype=jnp.int32)
    key = rotate(head_norm(key_raw, k_norm_gain), positions).astype(jnp.bfloat16)
    value_rows = value_raw.astype(jnp.bfloat16)
    joined = jnp.concatenate([key, value_rows], axis=1)
    reach = (WINDOW - 1 + rows - 1) // rows
    earlier = [shifted(joined, TOK, offset) for offset in range(reach, 0, -1)]
    normed_late, _ = lax.optimization_barrier((normed, joined))
    query_raw = jnp.einsum(
        "jrc,jcn->rn", normed_late, weights3[:, :, :width_query], preferred_element_type=jnp.float32
    )
    query = rotate(head_norm(query_raw, q_norm_gain), positions).astype(jnp.bfloat16)
    window_kv = jnp.concatenate(earlier + [joined], axis=0)
    window_extent = window_kv.shape[0]
    key_pos = (tok_index - reach) * rows + jnp.arange(window_extent, dtype=jnp.int32)
    kv_heads = width_kv // HEAD_SIZE
    query_group_count = width_query // HEAD_SIZE // kv_heads
    query_four_axes = query.reshape(rows, kv_heads, query_group_count, HEAD_SIZE)
    keys_three_axes = window_kv[:, :width_kv].reshape(window_extent, kv_heads, HEAD_SIZE)
    values_three_axes = window_kv[:, width_kv:].reshape(window_extent, kv_heads, HEAD_SIZE)
    scores = (
        jnp.einsum(
            "tkgd,skd->kgts", query_four_axes, keys_three_axes, preferred_element_type=jnp.float32
        )
        * score_scale
    )
    allowed = (
        (key_pos[None, :] <= positions[:, None])
        & (key_pos[None, :] > positions[:, None] - WINDOW)
        & (key_pos[None, :] >= 0)
    )
    masked = jnp.where(allowed, scores, -1e30)
    top = jnp.max(masked, axis=-1, keepdims=True)
    weights = jnp.where(allowed, jnp.exp(masked - top), 0.0)
    total = jnp.sum(weights, axis=-1)
    probs = weights.astype(jnp.bfloat16)
    mixed = jnp.einsum(
        "kgts,skd->tkgd", probs, values_three_axes, preferred_element_type=jnp.float32
    )
    mixed = mixed / jnp.transpose(total, (2, 0, 1))[..., None]
    heads_out = mixed.reshape(rows, width_query).astype(jnp.bfloat16)
    n_y, n_c = lax.axis_size("hy"), lax.axis_size("hc")
    by_core = w_out.reshape(w_out.shape[0], n_y, n_c, -1).transpose(0, 2, 1, 3)
    partial_value = jnp.dot(
        heads_out, by_core.reshape(w_out.shape), preferred_element_type=jnp.float32
    )
    on_chip = lax.psum_scatter(
        partial_value.astype(jnp.bfloat16), "hc", scatter_dimension=1, tiled=True
    )
    return lax.psum_scatter(on_chip, "hy", scatter_dimension=1, tiled=True)


def solution(mesh):
    devices = mesh.devices
    n_x = len({d.coords[0] for d in devices.flat})
    n_y = len({d.coords[1] for d in devices.flat})
    split = jax.sharding.Mesh(
        devices.reshape(n_x, devices.shape[0] // n_x, n_y, devices.shape[1] // n_y),
        ("tx", "tz", "hy", "hc"),
    )
    in_specs = (
        P(TOK, HID),
        P(None, HID),
        P(TOK, HID),
        P(TOK, HID),
        P(TOK, HID),
        P(),
        P(),
        P(HID, None),
    )
    out_specs = P(TOK, HID)
    return jax.shard_map(local, mesh=split, in_specs=in_specs, out_specs=out_specs, check_vma=False)
```

```python
import math

import jax
import jax.numpy as jnp
from jax import lax
from jax.sharding import PartitionSpec as P

HEAD_SIZE = 128
WINDOW = 1024


score_scale = 168.0 ** (-0.5)


def shifted(value, axis, steps):
    count = lax.axis_size(axis)
    leading, last = (max(0, -steps), min(count, count - steps))
    return lax.ppermute(value, axis, [(source, source + steps) for source in range(leading, last)])


def head_norm(field, gain):
    count = field.shape[0]
    heads = field.reshape(count, -1, HEAD_SIZE)
    mean_square = jnp.mean(heads * heads, axis=-1, keepdims=True)
    scaled = (
        heads * lax.rsqrt(mean_square + 1e-06) * gain.astype(jnp.float32).reshape(1, 1, HEAD_SIZE)
    )
    return scaled.reshape(count, -1)


def rotate(field, positions):
    count = field.shape[0]
    heads = field.reshape(count, -1, HEAD_SIZE)
    half = HEAD_SIZE // 2
    inverse = jnp.exp(-math.log(10000.0) * jnp.arange(half, dtype=jnp.float32) * 2.0 / HEAD_SIZE)
    angles = positions.astype(jnp.float32)[:, None] * inverse[None, :]
    cosine = jnp.cos(angles)[:, None, :]
    sine = jnp.sin(angles)[:, None, :]
    first = heads[..., :half]
    second = heads[..., half:]
    turned = jnp.concatenate(
        [first * cosine - second * sine, second * cosine + first * sine], axis=-1
    )
    return turned.reshape(count, -1)


def local(tokens, norm_gain, w_query, w_key, value_matrix, q_norm_gain, k_norm_gain, w_out):
    rows = tokens.shape[0]
    with_gain = jnp.concatenate([tokens, norm_gain], axis=0)
    n_hid = lax.axis_size("hid")
    hid_index = lax.axis_index("hid")
    received = [with_gain] + [
        lax.ppermute(with_gain, "hid", [(i, (i + k) % n_hid) for i in range(n_hid)])
        for k in range(1, n_hid)
    ]
    by_shift = jnp.stack(received)
    ordered = jnp.take(by_shift, (hid_index - jnp.arange(n_hid)) % n_hid, axis=0)
    values32 = ordered[:, :rows].astype(jnp.float32)
    gain_rows = ordered[:, rows:].astype(jnp.float32)
    mean_square = jnp.sum(values32 * values32, axis=(0, 2)) / (n_hid * values32.shape[2])
    scale_rows = lax.rsqrt(mean_square + 1e-06)[None, :, None]
    normed = (values32 * scale_rows * gain_rows).astype(jnp.bfloat16)
    width_query = w_query.shape[1]
    width_kv = w_key.shape[1]
    stacked = lax.all_gather(
        jnp.concatenate([w_query, w_key, value_matrix], axis=1), "tok", axis=0, tiled=True
    )
    weights3 = stacked.reshape(n_hid, normed.shape[2], stacked.shape[1])
    projected_kv = jnp.einsum(
        "jrc,jcn->rn", normed, weights3[:, :, width_query:], preferred_element_type=jnp.float32
    )
    key_raw = projected_kv[:, :width_kv]
    value_raw = projected_kv[:, width_kv:]
    tok_index = lax.axis_index("tok")
    positions = tok_index * rows + jnp.arange(rows, dtype=jnp.int32)
    key = rotate(head_norm(key_raw, k_norm_gain), positions).astype(jnp.bfloat16)
    value_rows = value_raw.astype(jnp.bfloat16)
    reach = (WINDOW - 1 + rows - 1) // rows
    earlier_keys = [shifted(key, "tok", offset) for offset in range(reach, 0, -1)]
    earlier_values = [shifted(value_rows, "tok", offset) for offset in range(reach, 0, -1)]
    normed_late, _ = lax.optimization_barrier((normed, earlier_keys[0]))
    query_raw = jnp.einsum(
        "jrc,jcn->rn", normed_late, weights3[:, :, :width_query], preferred_element_type=jnp.float32
    )
    query = rotate(head_norm(query_raw, q_norm_gain), positions).astype(jnp.bfloat16)
    window_keys = jnp.concatenate(earlier_keys + [key], axis=0)
    window_values = jnp.concatenate(earlier_values + [value_rows], axis=0)
    window_extent = window_keys.shape[0]
    key_pos = (tok_index - reach) * rows + jnp.arange(window_extent, dtype=jnp.int32)
    kv_heads = width_kv // HEAD_SIZE
    query_group_count = width_query // HEAD_SIZE // kv_heads
    query_four_axes = query.reshape(rows, kv_heads, query_group_count, HEAD_SIZE)
    keys_three_axes = window_keys.reshape(window_extent, kv_heads, HEAD_SIZE)
    values_three_axes = window_values.reshape(window_extent, kv_heads, HEAD_SIZE)
    scores = (
        jnp.einsum(
            "tkgd,skd->kgts", query_four_axes, keys_three_axes, preferred_element_type=jnp.float32
        )
        * score_scale
    )
    allowed = (
        (key_pos[None, :] <= positions[:, None])
        & (key_pos[None, :] > positions[:, None] - WINDOW)
        & (key_pos[None, :] >= 0)
    )
    masked = jnp.where(allowed, scores, -1e30)
    top = jnp.max(masked, axis=-1, keepdims=True)
    weights = jnp.where(allowed, jnp.exp(masked - top), 0.0)
    total = jnp.sum(weights, axis=-1)
    probs = weights.astype(jnp.bfloat16)
    mixed = jnp.einsum(
        "kgts,skd->tkgd", probs, values_three_axes, preferred_element_type=jnp.float32
    )
    mixed = mixed / jnp.transpose(total, (2, 0, 1))[..., None]
    heads_out = mixed.reshape(rows, width_query).astype(jnp.bfloat16)
    partial_value = jnp.dot(heads_out, w_out, preferred_element_type=jnp.float32)
    return lax.psum_scatter(
        partial_value.astype(jnp.bfloat16), "hid", scatter_dimension=1, tiled=True
    )


def solution(mesh):
    in_specs = (
        P("tok", "hid"),
        P(None, "hid"),
        P("tok", "hid"),
        P("tok", "hid"),
        P("tok", "hid"),
        P(),
        P(),
        P("hid", None),
    )
    out_specs = P("tok", "hid")
    return jax.shard_map(local, mesh=mesh, in_specs=in_specs, out_specs=out_specs, check_vma=False)
```

```python
import math

import jax
import jax.numpy as jnp
from jax import lax
from jax.sharding import PartitionSpec as P

HEAD_SIZE = 128
WINDOW = 1024


score_scale = 168.0 ** (-0.5)


def shifted(value, axis, steps):
    count = lax.axis_size(axis)
    leading, last = (max(0, -steps), min(count, count - steps))
    return lax.ppermute(value, axis, [(source, source + steps) for source in range(leading, last)])


def head_norm(field, gain):
    count = field.shape[0]
    heads = field.reshape(count, -1, HEAD_SIZE)
    mean_square = jnp.mean(heads * heads, axis=-1, keepdims=True)
    scaled = (
        heads * lax.rsqrt(mean_square + 1e-06) * gain.astype(jnp.float32).reshape(1, 1, HEAD_SIZE)
    )
    return scaled.reshape(count, -1)


def rotate(field, positions):
    count = field.shape[0]
    heads = field.reshape(count, -1, HEAD_SIZE)
    half = HEAD_SIZE // 2
    inverse = jnp.exp(-math.log(10000.0) * jnp.arange(half, dtype=jnp.float32) * 2.0 / HEAD_SIZE)
    angles = positions.astype(jnp.float32)[:, None] * inverse[None, :]
    cosine = jnp.cos(angles)[:, None, :]
    sine = jnp.sin(angles)[:, None, :]
    first = heads[..., :half]
    second = heads[..., half:]
    turned = jnp.concatenate(
        [first * cosine - second * sine, second * cosine + first * sine], axis=-1
    )
    return turned.reshape(count, -1)


def local(tokens, norm_gain, w_query, w_key, value_matrix, q_norm_gain, k_norm_gain, w_out):
    rows = tokens.shape[0]
    with_gain = jnp.concatenate([tokens, norm_gain], axis=0)
    n_hid = lax.axis_size("hid")
    hid_index = lax.axis_index("hid")
    received = [with_gain] + [
        lax.ppermute(with_gain, "hid", [(i, (i + k) % n_hid) for i in range(n_hid)])
        for k in range(1, n_hid)
    ]
    by_shift = jnp.stack(received)
    ordered = jnp.take(by_shift, (hid_index - jnp.arange(n_hid)) % n_hid, axis=0)
    values32 = ordered[:, :rows].astype(jnp.float32)
    gain_rows = ordered[:, rows:].astype(jnp.float32)
    mean_square = jnp.sum(values32 * values32, axis=(0, 2)) / (n_hid * values32.shape[2])
    scale_rows = lax.rsqrt(mean_square + 1e-06)[None, :, None]
    normed = (values32 * scale_rows * gain_rows).astype(jnp.bfloat16)
    width_query = w_query.shape[1]
    width_kv = w_key.shape[1]
    stacked = lax.all_gather(
        jnp.concatenate([w_query, w_key, value_matrix], axis=1), "tok", axis=0, tiled=True
    )
    weights3 = stacked.reshape(n_hid, normed.shape[2], stacked.shape[1])
    tok_index = lax.axis_index("tok")
    positions = tok_index * rows + jnp.arange(rows, dtype=jnp.int32)
    reach = (WINDOW - 1 + rows - 1) // rows
    key_raw = jnp.einsum(
        "jrc,jcn->rn",
        normed,
        weights3[:, :, width_query : width_query + width_kv],
        preferred_element_type=jnp.float32,
    )
    key = rotate(head_norm(key_raw, k_norm_gain), positions).astype(jnp.bfloat16)
    earlier_keys = [shifted(key, "tok", offset) for offset in range(reach, 0, -1)]
    normed_mid, _ = lax.optimization_barrier((normed, earlier_keys[0]))
    value_raw = jnp.einsum(
        "jrc,jcn->rn",
        normed_mid,
        weights3[:, :, width_query + width_kv :],
        preferred_element_type=jnp.float32,
    )
    value_rows = value_raw.astype(jnp.bfloat16)
    earlier_values = [shifted(value_rows, "tok", offset) for offset in range(reach, 0, -1)]
    normed_late, _ = lax.optimization_barrier((normed_mid, earlier_values[0]))
    query_raw = jnp.einsum(
        "jrc,jcn->rn", normed_late, weights3[:, :, :width_query], preferred_element_type=jnp.float32
    )
    query = rotate(head_norm(query_raw, q_norm_gain), positions).astype(jnp.bfloat16)
    window_keys = jnp.concatenate(earlier_keys + [key], axis=0)
    window_values = jnp.concatenate(earlier_values + [value_rows], axis=0)
    window_extent = window_keys.shape[0]
    key_pos = (tok_index - reach) * rows + jnp.arange(window_extent, dtype=jnp.int32)
    kv_heads = width_kv // HEAD_SIZE
    query_group_count = width_query // HEAD_SIZE // kv_heads
    query_four_axes = query.reshape(rows, kv_heads, query_group_count, HEAD_SIZE)
    keys_three_axes = window_keys.reshape(window_extent, kv_heads, HEAD_SIZE)
    values_three_axes = window_values.reshape(window_extent, kv_heads, HEAD_SIZE)
    scores = (
        jnp.einsum(
            "tkgd,skd->kgts", query_four_axes, keys_three_axes, preferred_element_type=jnp.float32
        )
        * score_scale
    )
    allowed = (
        (key_pos[None, :] <= positions[:, None])
        & (key_pos[None, :] > positions[:, None] - WINDOW)
        & (key_pos[None, :] >= 0)
    )
    masked = jnp.where(allowed, scores, -1e30)
    top = jnp.max(masked, axis=-1, keepdims=True)
    weights = jnp.where(allowed, jnp.exp(masked - top), 0.0)
    total = jnp.sum(weights, axis=-1)
    probs = weights.astype(jnp.bfloat16)
    mixed = jnp.einsum(
        "kgts,skd->tkgd", probs, values_three_axes, preferred_element_type=jnp.float32
    )
    mixed = mixed / jnp.transpose(total, (2, 0, 1))[..., None]
    heads_out = mixed.reshape(rows, width_query).astype(jnp.bfloat16)
    partial_value = jnp.dot(heads_out, w_out, preferred_element_type=jnp.float32)
    return lax.psum_scatter(
        partial_value.astype(jnp.bfloat16), "hid", scatter_dimension=1, tiled=True
    )


def solution(mesh):
    in_specs = (
        P("tok", "hid"),
        P(None, "hid"),
        P("tok", "hid"),
        P("tok", "hid"),
        P("tok", "hid"),
        P(),
        P(),
        P("hid", None),
    )
    out_specs = P("tok", "hid")
    return jax.shard_map(local, mesh=mesh, in_specs=in_specs, out_specs=out_specs, check_vma=False)
```

```python
import math

import jax
import jax.numpy as jnp
from jax import lax
from jax.sharding import PartitionSpec as P

HEAD_SIZE = 128
WINDOW = 1024


score_scale = 168.0 ** (-0.5)


def shifted(value, axis, steps):
    count = lax.axis_size(axis)
    leading, last = (max(0, -steps), min(count, count - steps))
    return lax.ppermute(value, axis, [(source, source + steps) for source in range(leading, last)])


def head_norm(field, gain):
    count = field.shape[0]
    heads = field.reshape(count, -1, HEAD_SIZE)
    mean_square = jnp.mean(heads * heads, axis=-1, keepdims=True)
    scaled = (
        heads * lax.rsqrt(mean_square + 1e-06) * gain.astype(jnp.float32).reshape(1, 1, HEAD_SIZE)
    )
    return scaled.reshape(count, -1)


def rotate(field, positions):
    count = field.shape[0]
    heads = field.reshape(count, -1, HEAD_SIZE)
    half = HEAD_SIZE // 2
    inverse = jnp.exp(-math.log(10000.0) * jnp.arange(half, dtype=jnp.float32) * 2.0 / HEAD_SIZE)
    angles = positions.astype(jnp.float32)[:, None] * inverse[None, :]
    cosine = jnp.cos(angles)[:, None, :]
    sine = jnp.sin(angles)[:, None, :]
    first = heads[..., :half]
    second = heads[..., half:]
    turned = jnp.concatenate(
        [first * cosine - second * sine, second * cosine + first * sine], axis=-1
    )
    return turned.reshape(count, -1)


def local(tokens, norm_gain, w_query, w_key, value_matrix, q_norm_gain, k_norm_gain, w_out):
    rows = tokens.shape[0]
    with_gain = jnp.concatenate([tokens, norm_gain], axis=0)
    n_hid = lax.axis_size("hid")
    hid_index = lax.axis_index("hid")
    received = [with_gain] + [
        lax.ppermute(with_gain, "hid", [(i, (i + k) % n_hid) for i in range(n_hid)])
        for k in range(1, n_hid)
    ]
    by_shift = jnp.stack(received)
    ordered = jnp.take(by_shift, (hid_index - jnp.arange(n_hid)) % n_hid, axis=0)
    values32 = ordered[:, :rows].astype(jnp.float32)
    gain_rows = ordered[:, rows:].astype(jnp.float32)
    mean_square = jnp.sum(values32 * values32, axis=(0, 2)) / (n_hid * values32.shape[2])
    scale_rows = lax.rsqrt(mean_square + 1e-06)[None, :, None]
    normed = (values32 * scale_rows * gain_rows).astype(jnp.bfloat16)
    width_query = w_query.shape[1]
    width_kv = w_key.shape[1]
    stacked = lax.all_gather(
        jnp.concatenate([w_query, w_key, value_matrix], axis=1), "tok", axis=0, tiled=True
    )
    weights3 = stacked.reshape(n_hid, normed.shape[2], stacked.shape[1])
    tok_index = lax.axis_index("tok")
    positions = tok_index * rows + jnp.arange(rows, dtype=jnp.int32)
    reach = (WINDOW - 1 + rows - 1) // rows
    key_pos = (tok_index - reach) * rows + jnp.arange((reach + 1) * rows, dtype=jnp.int32)
    allowed = (
        (key_pos[None, :] <= positions[:, None])
        & (key_pos[None, :] > positions[:, None] - WINDOW)
        & (key_pos[None, :] >= 0)
    )
    allowed, normed = lax.optimization_barrier((allowed, normed))
    projected_kv = jnp.einsum(
        "jrc,jcn->rn", normed, weights3[:, :, width_query:], preferred_element_type=jnp.float32
    )
    key_raw = projected_kv[:, :width_kv]
    value_raw = projected_kv[:, width_kv:]
    key = rotate(head_norm(key_raw, k_norm_gain), positions).astype(jnp.bfloat16)
    value_rows = value_raw.astype(jnp.bfloat16)
    earlier_keys = [shifted(key, "tok", offset) for offset in range(reach, 0, -1)]
    earlier_values = [shifted(value_rows, "tok", offset) for offset in range(reach, 0, -1)]
    normed_late, _ = lax.optimization_barrier((normed, earlier_keys[0]))
    query_raw = jnp.einsum(
        "jrc,jcn->rn", normed_late, weights3[:, :, :width_query], preferred_element_type=jnp.float32
    )
    query = rotate(head_norm(query_raw, q_norm_gain), positions).astype(jnp.bfloat16)
    window_keys = jnp.concatenate(earlier_keys + [key], axis=0)
    window_values = jnp.concatenate(earlier_values + [value_rows], axis=0)
    window_extent = window_keys.shape[0]
    kv_heads = width_kv // HEAD_SIZE
    query_group_count = width_query // HEAD_SIZE // kv_heads
    query_four_axes = query.reshape(rows, kv_heads, query_group_count, HEAD_SIZE)
    keys_three_axes = window_keys.reshape(window_extent, kv_heads, HEAD_SIZE)
    values_three_axes = window_values.reshape(window_extent, kv_heads, HEAD_SIZE)
    scores = (
        jnp.einsum(
            "tkgd,skd->kgts", query_four_axes, keys_three_axes, preferred_element_type=jnp.float32
        )
        * score_scale
    )
    masked = jnp.where(allowed, scores, -1e30)
    top = jnp.max(masked, axis=-1, keepdims=True)
    weights = jnp.where(allowed, jnp.exp(masked - top), 0.0)
    total = jnp.sum(weights, axis=-1)
    probs = weights.astype(jnp.bfloat16)
    mixed = jnp.einsum(
        "kgts,skd->tkgd", probs, values_three_axes, preferred_element_type=jnp.float32
    )
    mixed = mixed / jnp.transpose(total, (2, 0, 1))[..., None]
    heads_out = mixed.reshape(rows, width_query).astype(jnp.bfloat16)
    partial_value = jnp.dot(heads_out, w_out, preferred_element_type=jnp.float32)
    return lax.psum_scatter(
        partial_value.astype(jnp.bfloat16), "hid", scatter_dimension=1, tiled=True
    )


def solution(mesh):
    in_specs = (
        P("tok", "hid"),
        P(None, "hid"),
        P("tok", "hid"),
        P("tok", "hid"),
        P("tok", "hid"),
        P(),
        P(),
        P("hid", None),
    )
    out_specs = P("tok", "hid")
    return jax.shard_map(local, mesh=mesh, in_specs=in_specs, out_specs=out_specs, check_vma=False)
```

```python
import math

import jax
import jax.numpy as jnp
from jax import lax
from jax.sharding import PartitionSpec as P

HEAD_SIZE = 128
WINDOW = 1024


score_scale = 168.0 ** (-0.5)


def shifted(value, axis, steps):
    count = lax.axis_size(axis)
    leading, last = (max(0, -steps), min(count, count - steps))
    return lax.ppermute(value, axis, [(source, source + steps) for source in range(leading, last)])


def head_norm(field, gain):
    count = field.shape[0]
    heads = field.reshape(count, -1, HEAD_SIZE)
    mean_square = jnp.mean(heads * heads, axis=-1, keepdims=True)
    scaled = (
        heads * lax.rsqrt(mean_square + 1e-06) * gain.astype(jnp.float32).reshape(1, 1, HEAD_SIZE)
    )
    return scaled.reshape(count, -1)


def rotate(field, positions):
    count = field.shape[0]
    heads = field.reshape(count, -1, HEAD_SIZE)
    half = HEAD_SIZE // 2
    inverse = jnp.exp(-math.log(10000.0) * jnp.arange(half, dtype=jnp.float32) * 2.0 / HEAD_SIZE)
    angles = positions.astype(jnp.float32)[:, None] * inverse[None, :]
    cosine = jnp.cos(angles)[:, None, :]
    sine = jnp.sin(angles)[:, None, :]
    first = heads[..., :half]
    second = heads[..., half:]
    turned = jnp.concatenate(
        [first * cosine - second * sine, second * cosine + first * sine], axis=-1
    )
    return turned.reshape(count, -1)


def local(tokens, norm_gain, w_query, w_key, value_matrix, q_norm_gain, k_norm_gain, w_out):
    rows = tokens.shape[0]
    with_gain = jnp.concatenate([tokens, norm_gain], axis=0)
    n_hid = lax.axis_size("hid")
    hid_index = lax.axis_index("hid")
    received = [with_gain] + [
        lax.ppermute(with_gain, "hid", [(i, (i + k) % n_hid) for i in range(n_hid)])
        for k in range(1, n_hid)
    ]
    by_shift = jnp.stack(received)
    ordered = jnp.take(by_shift, (hid_index - jnp.arange(n_hid)) % n_hid, axis=0)
    values32 = ordered[:, :rows].astype(jnp.float32)
    gain_rows = ordered[:, rows:].astype(jnp.float32)
    mean_square = jnp.sum(values32 * values32, axis=(0, 2)) / (n_hid * values32.shape[2])
    scale_rows = lax.rsqrt(mean_square + 1e-06)[None, :, None]
    normed = (values32 * scale_rows * gain_rows).astype(jnp.bfloat16)
    width_query = w_query.shape[1]
    width_kv = w_key.shape[1]
    stacked = lax.all_gather(
        jnp.concatenate([w_query, w_key, value_matrix], axis=1), "tok", axis=0, tiled=True
    )
    weights3 = stacked.reshape(n_hid, normed.shape[2], stacked.shape[1])
    tok_index = lax.axis_index("tok")
    positions = tok_index * rows + jnp.arange(rows, dtype=jnp.int32)
    reach = (WINDOW - 1 + rows - 1) // rows
    key_pos = (tok_index - reach) * rows + jnp.arange((reach + 1) * rows, dtype=jnp.int32)
    allowed = (
        (key_pos[None, :] <= positions[:, None])
        & (key_pos[None, :] > positions[:, None] - WINDOW)
        & (key_pos[None, :] >= 0)
    )
    allowed, normed = lax.optimization_barrier((allowed, normed))
    key_raw = jnp.einsum(
        "jrc,jcn->rn",
        normed,
        weights3[:, :, width_query : width_query + width_kv],
        preferred_element_type=jnp.float32,
    )
    key = rotate(head_norm(key_raw, k_norm_gain), positions).astype(jnp.bfloat16)
    earlier_keys = [shifted(key, "tok", offset) for offset in range(1, reach + 1)][::-1]
    normed_mid, _ = lax.optimization_barrier((normed, key))
    value_raw = jnp.einsum(
        "jrc,jcn->rn",
        normed_mid,
        weights3[:, :, width_query + width_kv :],
        preferred_element_type=jnp.float32,
    )
    value_rows = value_raw.astype(jnp.bfloat16)
    earlier_values = [shifted(value_rows, "tok", offset) for offset in range(reach, 0, -1)]
    normed_late, _ = lax.optimization_barrier((normed_mid, value_rows))
    query_raw = jnp.einsum(
        "jrc,jcn->rn", normed_late, weights3[:, :, :width_query], preferred_element_type=jnp.float32
    )
    query = rotate(head_norm(query_raw, q_norm_gain), positions).astype(jnp.bfloat16)
    window_keys = jnp.concatenate(earlier_keys + [key], axis=0)
    window_values = jnp.concatenate(earlier_values + [value_rows], axis=0)
    window_extent = window_keys.shape[0]
    kv_heads = width_kv // HEAD_SIZE
    query_group_count = width_query // HEAD_SIZE // kv_heads
    query_four_axes = query.reshape(rows, kv_heads, query_group_count, HEAD_SIZE)
    keys_three_axes = window_keys.reshape(window_extent, kv_heads, HEAD_SIZE)
    values_three_axes = window_values.reshape(window_extent, kv_heads, HEAD_SIZE)
    scores = (
        jnp.einsum(
            "tkgd,skd->kgts", query_four_axes, keys_three_axes, preferred_element_type=jnp.float32
        )
        * score_scale
    )
    masked = jnp.where(allowed, scores, -1e30)
    top = jnp.max(masked, axis=-1, keepdims=True)
    weights = jnp.where(allowed, jnp.exp(masked - top), 0.0)
    total = jnp.sum(weights, axis=-1)
    probs = weights.astype(jnp.bfloat16)
    mixed = jnp.einsum(
        "kgts,skd->tkgd", probs, values_three_axes, preferred_element_type=jnp.float32
    )
    mixed = mixed / jnp.transpose(total, (2, 0, 1))[..., None]
    heads_out = mixed.reshape(rows, width_query).astype(jnp.bfloat16)
    partial_value = jnp.dot(heads_out, w_out, preferred_element_type=jnp.float32)
    return lax.psum_scatter(
        partial_value.astype(jnp.bfloat16), "hid", scatter_dimension=1, tiled=True
    )


def solution(mesh):
    in_specs = (
        P("tok", "hid"),
        P(None, "hid"),
        P("tok", "hid"),
        P("tok", "hid"),
        P("tok", "hid"),
        P(),
        P(),
        P("hid", None),
    )
    out_specs = P("tok", "hid")
    return jax.shard_map(local, mesh=mesh, in_specs=in_specs, out_specs=out_specs, check_vma=False)
```

```python
import math

import jax
import jax.numpy as jnp
from jax import lax
from jax.sharding import PartitionSpec as P

HEAD_SIZE = 128
WINDOW = 1024


score_scale = 168.0 ** (-0.5)


def shifted(value, axis, steps):
    count = lax.axis_size(axis)
    leading, last = (max(0, -steps), min(count, count - steps))
    return lax.ppermute(value, axis, [(source, source + steps) for source in range(leading, last)])


def head_norm(field, gain):
    count = field.shape[0]
    heads = field.reshape(count, -1, HEAD_SIZE)
    mean_square = jnp.mean(heads * heads, axis=-1, keepdims=True)
    scaled = (
        heads * lax.rsqrt(mean_square + 1e-06) * gain.astype(jnp.float32).reshape(1, 1, HEAD_SIZE)
    )
    return scaled.reshape(count, -1)


def rotate(field, positions):
    count = field.shape[0]
    heads = field.reshape(count, -1, HEAD_SIZE)
    half = HEAD_SIZE // 2
    inverse = jnp.exp(-math.log(10000.0) * jnp.arange(half, dtype=jnp.float32) * 2.0 / HEAD_SIZE)
    angles = positions.astype(jnp.float32)[:, None] * inverse[None, :]
    cosine = jnp.cos(angles)[:, None, :]
    sine = jnp.sin(angles)[:, None, :]
    first = heads[..., :half]
    second = heads[..., half:]
    turned = jnp.concatenate(
        [first * cosine - second * sine, second * cosine + first * sine], axis=-1
    )
    return turned.reshape(count, -1)


def local(tokens, norm_gain, w_query, w_key, value_matrix, q_norm_gain, k_norm_gain, w_out):
    rows = tokens.shape[0]
    with_gain = jnp.concatenate([tokens, norm_gain], axis=0)
    n_hid = lax.axis_size("hid")
    hid_index = lax.axis_index("hid")
    received = [with_gain] + [
        lax.ppermute(with_gain, "hid", [(i, (i + k) % n_hid) for i in range(n_hid)])
        for k in range(1, n_hid)
    ]
    by_shift = jnp.stack(received)
    ordered = jnp.take(by_shift, (hid_index - jnp.arange(n_hid)) % n_hid, axis=0)
    values32 = ordered[:, :rows].astype(jnp.float32)
    gain_rows = ordered[:, rows:].astype(jnp.float32)
    mean_square = jnp.sum(values32 * values32, axis=(0, 2)) / (n_hid * values32.shape[2])
    scale_rows = lax.rsqrt(mean_square + 1e-06)[None, :, None]
    normed = (values32 * scale_rows * gain_rows).astype(jnp.bfloat16)
    width_query = w_query.shape[1]
    width_kv = w_key.shape[1]
    stacked = lax.all_gather(
        jnp.concatenate([w_query, w_key, value_matrix], axis=1), "tok", axis=0, tiled=True
    )
    weights3 = stacked.reshape(n_hid, normed.shape[2], stacked.shape[1])
    projected_kv = jnp.einsum(
        "jrc,jcn->rn", normed, weights3[:, :, width_query:], preferred_element_type=jnp.float32
    )
    key_raw = projected_kv[:, :width_kv]
    value_raw = projected_kv[:, width_kv:]
    tok_index = lax.axis_index("tok")
    positions = tok_index * rows + jnp.arange(rows, dtype=jnp.int32)
    key = rotate(head_norm(key_raw, k_norm_gain), positions).astype(jnp.bfloat16)
    value_rows = value_raw.astype(jnp.bfloat16)
    reach = (WINDOW - 1 + rows - 1) // rows
    far = [shifted(jnp.concatenate([key, value_rows], axis=1), "tok", offset) for offset in range(reach, 1, -1)]
    earlier_keys = [block[:, :width_kv] for block in far] + [shifted(key, "tok", 1)]
    earlier_values = [block[:, width_kv:] for block in far] + [shifted(value_rows, "tok", 1)]
    normed_late, _ = lax.optimization_barrier((normed, earlier_keys[0]))
    query_raw = jnp.einsum(
        "jrc,jcn->rn", normed_late, weights3[:, :, :width_query], preferred_element_type=jnp.float32
    )
    query = rotate(head_norm(query_raw, q_norm_gain), positions).astype(jnp.bfloat16)
    window_keys = jnp.concatenate(earlier_keys + [key], axis=0)
    window_values = jnp.concatenate(earlier_values + [value_rows], axis=0)
    window_extent = window_keys.shape[0]
    key_pos = (tok_index - reach) * rows + jnp.arange(window_extent, dtype=jnp.int32)
    kv_heads = width_kv // HEAD_SIZE
    query_group_count = width_query // HEAD_SIZE // kv_heads
    query_four_axes = query.reshape(rows, kv_heads, query_group_count, HEAD_SIZE)
    keys_three_axes = window_keys.reshape(window_extent, kv_heads, HEAD_SIZE)
    values_three_axes = window_values.reshape(window_extent, kv_heads, HEAD_SIZE)
    scores = (
        jnp.einsum(
            "tkgd,skd->kgts", query_four_axes, keys_three_axes, preferred_element_type=jnp.float32
        )
        * score_scale
    )
    allowed = (
        (key_pos[None, :] <= positions[:, None])
        & (key_pos[None, :] > positions[:, None] - WINDOW)
        & (key_pos[None, :] >= 0)
    )
    masked = jnp.where(allowed, scores, -1e30)
    top = jnp.max(masked, axis=-1, keepdims=True)
    weights = jnp.where(allowed, jnp.exp(masked - top), 0.0)
    total = jnp.sum(weights, axis=-1)
    probs = weights.astype(jnp.bfloat16)
    mixed = jnp.einsum(
        "kgts,skd->tkgd", probs, values_three_axes, preferred_element_type=jnp.float32
    )
    mixed = mixed / jnp.transpose(total, (2, 0, 1))[..., None]
    heads_out = mixed.reshape(rows, width_query).astype(jnp.bfloat16)
    partial_value = jnp.dot(heads_out, w_out, preferred_element_type=jnp.float32)
    return lax.psum_scatter(
        partial_value.astype(jnp.bfloat16), "hid", scatter_dimension=1, tiled=True
    )


def solution(mesh):
    in_specs = (
        P("tok", "hid"),
        P(None, "hid"),
        P("tok", "hid"),
        P("tok", "hid"),
        P("tok", "hid"),
        P(),
        P(),
        P("hid", None),
    )
    out_specs = P("tok", "hid")
    return jax.shard_map(local, mesh=mesh, in_specs=in_specs, out_specs=out_specs, check_vma=False)
```

```python
import math

import jax
import jax.numpy as jnp
from jax import lax
from jax.sharding import PartitionSpec as P

HEAD_SIZE = 128
WINDOW = 1024


score_scale = 168.0 ** (-0.5)


def shifted(value, axis, steps):
    count = lax.axis_size(axis)
    leading, last = (max(0, -steps), min(count, count - steps))
    return lax.ppermute(value, axis, [(source, source + steps) for source in range(leading, last)])


def head_norm(field, gain):
    count = field.shape[0]
    heads = field.reshape(count, -1, HEAD_SIZE)
    mean_square = jnp.mean(heads * heads, axis=-1, keepdims=True)
    scaled = (
        heads * lax.rsqrt(mean_square + 1e-06) * gain.astype(jnp.float32).reshape(1, 1, HEAD_SIZE)
    )
    return scaled.reshape(count, -1)


def rotate(field, positions):
    count = field.shape[0]
    heads = field.reshape(count, -1, HEAD_SIZE)
    half = HEAD_SIZE // 2
    inverse = jnp.exp(-math.log(10000.0) * jnp.arange(half, dtype=jnp.float32) * 2.0 / HEAD_SIZE)
    angles = positions.astype(jnp.float32)[:, None] * inverse[None, :]
    cosine = jnp.cos(angles)[:, None, :]
    sine = jnp.sin(angles)[:, None, :]
    first = heads[..., :half]
    second = heads[..., half:]
    turned = jnp.concatenate(
        [first * cosine - second * sine, second * cosine + first * sine], axis=-1
    )
    return turned.reshape(count, -1)


def local(tokens, norm_gain, w_query, w_key, value_matrix, q_norm_gain, k_norm_gain, w_out):
    rows = tokens.shape[0]
    with_gain = jnp.concatenate([tokens, norm_gain], axis=0)
    n_hid = lax.axis_size("hid")
    hid_index = lax.axis_index("hid")
    received = [with_gain] + [
        lax.ppermute(with_gain, "hid", [(i, (i + k) % n_hid) for i in range(n_hid)])
        for k in range(1, n_hid)
    ]
    by_shift = jnp.stack(received)
    ordered = jnp.take(by_shift, (hid_index - jnp.arange(n_hid)) % n_hid, axis=0)
    values32 = ordered[:, :rows].astype(jnp.float32)
    gain_rows = ordered[:, rows:].astype(jnp.float32)
    mean_square = jnp.sum(values32 * values32, axis=(0, 2)) / (n_hid * values32.shape[2])
    scale_rows = lax.rsqrt(mean_square + 1e-06)[None, :, None]
    normed = (values32 * scale_rows * gain_rows).astype(jnp.bfloat16)
    width_query = w_query.shape[1]
    width_kv = w_key.shape[1]
    stacked = lax.all_gather(
        jnp.concatenate([w_query, w_key, value_matrix], axis=1), "tok", axis=0, tiled=True
    )
    weights3 = stacked.reshape(n_hid, normed.shape[2], stacked.shape[1])
    projected_kv = jnp.einsum(
        "jrc,jcn->rn", normed, weights3[:, :, width_query:], preferred_element_type=jnp.float32
    )
    key_raw = projected_kv[:, :width_kv]
    value_raw = projected_kv[:, width_kv:]
    tok_index = lax.axis_index("tok")
    positions = tok_index * rows + jnp.arange(rows, dtype=jnp.int32)
    key = rotate(head_norm(key_raw, k_norm_gain), positions).astype(jnp.bfloat16)
    value_rows = value_raw.astype(jnp.bfloat16)
    reach = (WINDOW - 1 + rows - 1) // rows
    earlier_keys = [shifted(key, "tok", offset) for offset in range(reach, 0, -1)]
    earlier_values = [shifted(value_rows, "tok", offset) for offset in range(reach, 0, -1)]
    normed_late, _ = lax.optimization_barrier((normed, value_rows))
    query_raw = jnp.einsum(
        "jrc,jcn->rn", normed_late, weights3[:, :, :width_query], preferred_element_type=jnp.float32
    )
    query = rotate(head_norm(query_raw, q_norm_gain), positions).astype(jnp.bfloat16)
    window_keys = jnp.concatenate(earlier_keys + [key], axis=0)
    window_values = jnp.concatenate(earlier_values + [value_rows], axis=0)
    window_extent = window_keys.shape[0]
    key_pos = (tok_index - reach) * rows + jnp.arange(window_extent, dtype=jnp.int32)
    kv_heads = width_kv // HEAD_SIZE
    query_group_count = width_query // HEAD_SIZE // kv_heads
    query_four_axes = query.reshape(rows, kv_heads, query_group_count, HEAD_SIZE)
    keys_three_axes = window_keys.reshape(window_extent, kv_heads, HEAD_SIZE)
    values_three_axes = window_values.reshape(window_extent, kv_heads, HEAD_SIZE)
    scores = (
        jnp.einsum(
            "tkgd,skd->kgts", query_four_axes, keys_three_axes, preferred_element_type=jnp.float32
        )
        * score_scale
    )
    allowed = (
        (key_pos[None, :] <= positions[:, None])
        & (key_pos[None, :] > positions[:, None] - WINDOW)
        & (key_pos[None, :] >= 0)
    )
    masked = jnp.where(allowed, scores, -1e30)
    top = jnp.max(masked, axis=-1, keepdims=True)
    weights = jnp.where(allowed, jnp.exp(masked - top), 0.0)
    total = jnp.sum(weights, axis=-1)
    probs = weights.astype(jnp.bfloat16)
    mixed = jnp.einsum(
        "kgts,skd->tkgd", probs, values_three_axes, preferred_element_type=jnp.float32
    )
    mixed = mixed / jnp.transpose(total, (2, 0, 1))[..., None]
    heads_out = mixed.reshape(rows, width_query).astype(jnp.bfloat16)
    partial_value = jnp.dot(heads_out, w_out, preferred_element_type=jnp.float32)
    return lax.psum_scatter(
        partial_value.astype(jnp.bfloat16), "hid", scatter_dimension=1, tiled=True
    )


def solution(mesh):
    in_specs = (
        P("tok", "hid"),
        P(None, "hid"),
        P("tok", "hid"),
        P("tok", "hid"),
        P("tok", "hid"),
        P(),
        P(),
        P("hid", None),
    )
    out_specs = P("tok", "hid")
    return jax.shard_map(local, mesh=mesh, in_specs=in_specs, out_specs=out_specs, check_vma=False)
```

```python
import math

import jax
import jax.numpy as jnp
from jax import lax
from jax.sharding import PartitionSpec as P

HEAD_SIZE = 128
WINDOW = 1024


score_scale = 168.0 ** (-0.5)


def shifted(value, axis, steps):
    count = lax.axis_size(axis)
    leading, last = (max(0, -steps), min(count, count - steps))
    return lax.ppermute(value, axis, [(source, source + steps) for source in range(leading, last)])


def head_norm(field, gain):
    count = field.shape[0]
    heads = field.reshape(count, -1, HEAD_SIZE)
    mean_square = jnp.mean(heads * heads, axis=-1, keepdims=True)
    scaled = (
        heads * lax.rsqrt(mean_square + 1e-06) * gain.astype(jnp.float32).reshape(1, 1, HEAD_SIZE)
    )
    return scaled.reshape(count, -1)


def rotate(field, positions):
    count = field.shape[0]
    heads = field.reshape(count, -1, HEAD_SIZE)
    half = HEAD_SIZE // 2
    inverse = jnp.exp(-math.log(10000.0) * jnp.arange(half, dtype=jnp.float32) * 2.0 / HEAD_SIZE)
    angles = positions.astype(jnp.float32)[:, None] * inverse[None, :]
    cosine = jnp.cos(angles)[:, None, :]
    sine = jnp.sin(angles)[:, None, :]
    first = heads[..., :half]
    second = heads[..., half:]
    turned = jnp.concatenate(
        [first * cosine - second * sine, second * cosine + first * sine], axis=-1
    )
    return turned.reshape(count, -1)


def local(tokens, norm_gain, w_query, w_key, value_matrix, q_norm_gain, k_norm_gain, w_out):
    rows = tokens.shape[0]
    with_gain = jnp.concatenate([tokens, norm_gain], axis=0)
    n_hid = lax.axis_size("hid")
    hid_index = lax.axis_index("hid")
    received = [with_gain] + [
        lax.ppermute(with_gain, "hid", [(i, (i + k) % n_hid) for i in range(n_hid)])
        for k in range(1, n_hid)
    ]
    by_shift = jnp.stack(received)
    ordered = jnp.take(by_shift, (hid_index - jnp.arange(n_hid)) % n_hid, axis=0)
    values32 = ordered[:, :rows].astype(jnp.float32)
    gain_rows = ordered[:, rows:].astype(jnp.float32)
    mean_square = jnp.sum(values32 * values32, axis=(0, 2)) / (n_hid * values32.shape[2])
    scale_rows = lax.rsqrt(mean_square + 1e-06)[None, :, None]
    normed = (values32 * scale_rows * gain_rows).astype(jnp.bfloat16)
    width_query = w_query.shape[1]
    width_kv = w_key.shape[1]
    stacked = lax.all_gather(
        jnp.concatenate([w_query, w_key, value_matrix], axis=1), "tok", axis=0, tiled=True
    )
    weights3 = stacked.reshape(n_hid, normed.shape[2], stacked.shape[1])
    projected_kv = jnp.einsum(
        "jrc,jcn->rn", normed, weights3[:, :, width_query:], preferred_element_type=jnp.float32
    )
    key_raw = projected_kv[:, :width_kv]
    value_raw = projected_kv[:, width_kv:]
    tok_index = lax.axis_index("tok")
    positions = tok_index * rows + jnp.arange(rows, dtype=jnp.int32)
    key = rotate(head_norm(key_raw, k_norm_gain), positions).astype(jnp.bfloat16)
    value_rows = value_raw.astype(jnp.bfloat16)
    reach = (WINDOW - 1 + rows - 1) // rows
    earlier_keys = [shifted(key, "tok", offset) for offset in range(reach, 0, -1)]
    earlier_values = [shifted(value_rows, "tok", offset) for offset in range(reach, 0, -1)]
    normed_late, _ = lax.optimization_barrier((normed, value_rows))
    query_raw = jnp.einsum(
        "jrc,jcn->rn", normed_late, weights3[:, :, :width_query], preferred_element_type=jnp.float32
    )
    query = rotate(head_norm(query_raw, q_norm_gain), positions).astype(jnp.bfloat16)
    window_keys = jnp.concatenate(earlier_keys + [key], axis=0)
    window_values = jnp.concatenate(earlier_values + [value_rows], axis=0)
    window_extent = window_keys.shape[0]
    key_pos = (tok_index - reach) * rows + jnp.arange(window_extent, dtype=jnp.int32)
    kv_heads = width_kv // HEAD_SIZE
    query_group_count = width_query // HEAD_SIZE // kv_heads
    query_four_axes = query.reshape(rows, kv_heads, query_group_count, HEAD_SIZE)
    keys_three_axes = window_keys.reshape(window_extent, kv_heads, HEAD_SIZE)
    values_three_axes = window_values.reshape(window_extent, kv_heads, HEAD_SIZE)
    scores = (
        jnp.einsum(
            "tkgd,skd->kgts", query_four_axes, keys_three_axes, preferred_element_type=jnp.float32
        )
        * score_scale
    )
    allowed = (
        (key_pos[None, :] <= positions[:, None])
        & (key_pos[None, :] > positions[:, None] - WINDOW)
        & (key_pos[None, :] >= 0)
    )
    masked = jnp.where(allowed, scores, -1e30)
    top = jnp.max(masked, axis=-1, keepdims=True)
    weights = jnp.where(allowed, jnp.exp(masked - top), 0.0)
    total = jnp.sum(weights, axis=-1)
    probs = weights.astype(jnp.bfloat16)
    value_blocks = earlier_values + [value_rows]
    mixed = sum(
        jnp.einsum(
            "kgts,skd->tkgd",
            probs[..., index * rows : (index + 1) * rows],
            block.reshape(rows, kv_heads, HEAD_SIZE),
            preferred_element_type=jnp.float32,
        )
        for index, block in enumerate(value_blocks)
    )
    mixed = mixed / jnp.transpose(total, (2, 0, 1))[..., None]
    heads_out = mixed.reshape(rows, width_query).astype(jnp.bfloat16)
    partial_value = jnp.dot(heads_out, w_out, preferred_element_type=jnp.float32)
    return lax.psum_scatter(
        partial_value.astype(jnp.bfloat16), "hid", scatter_dimension=1, tiled=True
    )


def solution(mesh):
    in_specs = (
        P("tok", "hid"),
        P(None, "hid"),
        P("tok", "hid"),
        P("tok", "hid"),
        P("tok", "hid"),
        P(),
        P(),
        P("hid", None),
    )
    out_specs = P("tok", "hid")
    return jax.shard_map(local, mesh=mesh, in_specs=in_specs, out_specs=out_specs, check_vma=False)
```

```python
import math

import jax
import jax.numpy as jnp
from jax import lax
from jax.sharding import PartitionSpec as P

HEAD_SIZE = 128
WINDOW = 1024


score_scale = 168.0 ** (-0.5)


def shifted(value, axis, steps):
    count = lax.axis_size(axis)
    leading, last = (max(0, -steps), min(count, count - steps))
    return lax.ppermute(value, axis, [(source, source + steps) for source in range(leading, last)])


def head_norm(field, gain):
    count = field.shape[0]
    heads = field.reshape(count, -1, HEAD_SIZE)
    mean_square = jnp.mean(heads * heads, axis=-1, keepdims=True)
    scaled = (
        heads * lax.rsqrt(mean_square + 1e-06) * gain.astype(jnp.float32).reshape(1, 1, HEAD_SIZE)
    )
    return scaled.reshape(count, -1)


def rotate(field, positions):
    count = field.shape[0]
    heads = field.reshape(count, -1, HEAD_SIZE)
    half = HEAD_SIZE // 2
    inverse = jnp.exp(-math.log(10000.0) * jnp.arange(half, dtype=jnp.float32) * 2.0 / HEAD_SIZE)
    angles = positions.astype(jnp.float32)[:, None] * inverse[None, :]
    cosine = jnp.cos(angles)[:, None, :]
    sine = jnp.sin(angles)[:, None, :]
    first = heads[..., :half]
    second = heads[..., half:]
    turned = jnp.concatenate(
        [first * cosine - second * sine, second * cosine + first * sine], axis=-1
    )
    return turned.reshape(count, -1)


def local(tokens, norm_gain, w_query, w_key, value_matrix, q_norm_gain, k_norm_gain, w_out):
    rows = tokens.shape[0]
    with_gain = jnp.concatenate([tokens, norm_gain], axis=0)
    n_hid = lax.axis_size("hid")
    hid_index = lax.axis_index("hid")
    received = [with_gain] + [
        lax.ppermute(with_gain, "hid", [(i, (i + k) % n_hid) for i in range(n_hid)])
        for k in range(1, n_hid)
    ]
    by_shift = jnp.stack(received)
    ordered = jnp.take(by_shift, (hid_index - jnp.arange(n_hid)) % n_hid, axis=0)
    values32 = ordered[:, :rows].astype(jnp.float32)
    gain_rows = ordered[:, rows:].astype(jnp.float32)
    mean_square = jnp.sum(values32 * values32, axis=(0, 2)) / (n_hid * values32.shape[2])
    scale_rows = lax.rsqrt(mean_square + 1e-06)[None, :, None]
    normed = (values32 * scale_rows * gain_rows).astype(jnp.bfloat16)
    width_query = w_query.shape[1]
    width_kv = w_key.shape[1]
    stacked = lax.all_gather(
        jnp.concatenate([w_query, w_key, value_matrix], axis=1), "tok", axis=0, tiled=True
    )
    weights3 = stacked.reshape(n_hid, normed.shape[2], stacked.shape[1])
    projected_kv = jnp.einsum(
        "jrc,jcn->rn", normed, weights3[:, :, width_query:], preferred_element_type=jnp.float32
    )
    key_raw = projected_kv[:, :width_kv]
    value_raw = projected_kv[:, width_kv:]
    tok_index = lax.axis_index("tok")
    positions = tok_index * rows + jnp.arange(rows, dtype=jnp.int32)
    key = rotate(head_norm(key_raw, k_norm_gain), positions).astype(jnp.bfloat16)
    value_rows = value_raw.astype(jnp.bfloat16)
    reach = (WINDOW - 1 + rows - 1) // rows
    earlier_keys = [shifted(key, "tok", offset) for offset in range(reach, 0, -1)]
    earlier_values = [shifted(value_rows, "tok", offset) for offset in range(reach, 0, -1)]
    normed_late, _ = lax.optimization_barrier((normed, value_rows))
    query_raw = jnp.einsum(
        "jrc,jcn->rn", normed_late, weights3[:, :, :width_query], preferred_element_type=jnp.float32
    )
    query = rotate(head_norm(query_raw, q_norm_gain), positions).astype(jnp.bfloat16)
    window_keys = jnp.concatenate(earlier_keys + [key], axis=0)
    window_values = jnp.concatenate(earlier_values + [value_rows], axis=0)
    window_extent = window_keys.shape[0]
    key_pos = (tok_index - reach) * rows + jnp.arange(window_extent, dtype=jnp.int32)
    kv_heads = width_kv // HEAD_SIZE
    query_group_count = width_query // HEAD_SIZE // kv_heads
    query_four_axes = query.reshape(rows, kv_heads, query_group_count, HEAD_SIZE)
    keys_three_axes = window_keys.reshape(window_extent, kv_heads, HEAD_SIZE)
    values_three_axes = window_values.reshape(window_extent, kv_heads, HEAD_SIZE)
    scores = (
        jnp.einsum(
            "tkgd,skd->kgts", query_four_axes, keys_three_axes, preferred_element_type=jnp.float32
        )
        * score_scale
    )
    allowed = (
        (key_pos[None, :] <= positions[:, None])
        & (key_pos[None, :] > positions[:, None] - WINDOW)
        & (key_pos[None, :] >= 0)
    )
    masked = jnp.where(allowed, scores, -1e30)
    top = jnp.max(masked, axis=-1, keepdims=True)
    weights = jnp.where(allowed, jnp.exp(masked - top), 0.0)
    total = jnp.sum(weights, axis=-1)
    probs = weights.astype(jnp.bfloat16)
    first_block = earlier_values[0].reshape(rows, kv_heads, HEAD_SIZE)
    rest = jnp.concatenate(earlier_values[1:] + [value_rows], axis=0)
    mixed = jnp.einsum(
        "kgts,skd->tkgd", probs[..., :rows], first_block, preferred_element_type=jnp.float32
    ) + jnp.einsum(
        "kgts,skd->tkgd",
        probs[..., rows:],
        rest.reshape(window_extent - rows, kv_heads, HEAD_SIZE),
        preferred_element_type=jnp.float32,
    )
    mixed = mixed / jnp.transpose(total, (2, 0, 1))[..., None]
    heads_out = mixed.reshape(rows, width_query).astype(jnp.bfloat16)
    partial_value = jnp.dot(heads_out, w_out, preferred_element_type=jnp.float32)
    return lax.psum_scatter(
        partial_value.astype(jnp.bfloat16), "hid", scatter_dimension=1, tiled=True
    )


def solution(mesh):
    in_specs = (
        P("tok", "hid"),
        P(None, "hid"),
        P("tok", "hid"),
        P("tok", "hid"),
        P("tok", "hid"),
        P(),
        P(),
        P("hid", None),
    )
    out_specs = P("tok", "hid")
    return jax.shard_map(local, mesh=mesh, in_specs=in_specs, out_specs=out_specs, check_vma=False)
```
